256 devices in a mesh: seq: 32 (over y, x, core), tp: 8 (over z).
Axes of the slice: x: 4, y: 4, z: 8, core: 2. Of those that a mesh axis runs over, the one named last changes fastest.
Arguments:
- x_resid: bfloat16 [4096, 2880], P('seq', 'tp'), may hold values from -6 to 6
- q_new: bfloat16 [4096, 4096], P('seq', 'tp'), may hold values from -10 to 12
- kv_new: bfloat16 [4096, 8, 128], P('seq', 'tp'), may hold values from -4 to 4
- kv_cache: bfloat16 [1024, 32, 8, 128], P('seq', None, 'tp'), may hold values from -4 to 11.5
- cache_len: int32 [32], replicated, may hold values from 0 to 1024, as said below
- page_table: int32 [32, 32], replicated, may hold values from 0 to 1023, as said below
- sinks: float32 [64], P('tp'), may hold values from 0 to 8
- out_weight: bfloat16 [4096, 2880], P('tp'), may hold values from -0.09375 to 0.09375
- norm_gain: float32 [2880], replicated, may hold values from 0.1 to 1.9
- routes: int32 [4096, 4], P('seq'), may hold values from 0 to 31, all different within a row; in each aligned block of 128 rows (0 to 127, 128 to 255, ...) at most 32 rows name the same one
- route_wt: float32 [4096, 4], P('seq'), may hold values from 0.05 to 0.5
- w_gate: bfloat16 [32, 2880, 2880], P('seq', None, 'tp'), may hold values from -0.109375 to 0.109375
- w_up: bfloat16 [32, 2880, 2880], P('seq', None, 'tp'), may hold values from -0.109375 to 0.109375
- w_down: bfloat16 [32, 2880, 2880], P('seq', 'tp'), may hold values from -0.109375 to 0.109375
Outputs:
- attended: bfloat16 [4096, 4096], P('seq', 'tp')
- output: bfloat16 [4096, 2880], P('seq', 'tp')
The draws below stay inside these ranges and needn't reach their ends.
Inputs may be any that keep to these rules, and one draw needn't show every extreme that they name: `routes`: each row names 4 different experts; in each aligned block of 128 rows no expert is named by more than 32 rows. `cache_len`: the largest is exactly 1024. `page_table`: every pool page appears exactly once; pool pages d * 32 to (d + 1) * 32 - 1 hold exactly 1 pages of each request.
All inputs are finite; a program needn't handle non-finite values.
Results may differ from the reference program's by a relative error of at most 0.02.
Values may be sent and summed in bfloat16 or wider, within the bound.
No kernel may reach another device: no remote copies, remote signals or barrier semaphores. Data moves between devices by JAX's collectives and lax.ppermute only.
A program may use at most 128 MiB of HBM per device.

```python
import math
import jax
import jax.numpy as jnp
import numpy as np
from jax import lax

D = 2880
QH = 64
KVH = 8
HEAD = 64
EF = 2880
TOPK = 4
NEW = 128
MAXC = 1024
PAGE = 32
TOK_DEV = 128
EXPERTS = 32
TOKENS = 4096
REQUESTS = 32
MAXP = 32
SLOTS = 32
KPG = 1
CAP = 32
QPK = 8
N_SEQ = 32
N_TP = 8


def draw_q_new(key, part):
    first = jax.random.fold_in(key, 0)
    base = 2.5 * jnp.clip(jax.random.normal(first, (TOKENS, QH, HEAD), jnp.float32), -4.0, 4.0)
    return base.reshape(TOKENS, QH * HEAD).astype(jnp.bfloat16)


def draw_kv_cache(key, part):
    first = jax.random.fold_in(key, 0)
    pool = SLOTS * (MAXP // KPG)
    shape = (pool, PAGE, KVH, 2 * HEAD)
    base = jnp.clip(jax.random.normal(first, shape, jnp.float32), -4.0, 4.0)
    return base.astype(jnp.bfloat16)


def draw_cache_len(key, part):
    first, second, third = jax.random.split(key, 3)
    left = jax.random.randint(first, (REQUESTS,), 0, MAXC + 1)
    right = jax.random.randint(second, (REQUESTS,), 0, MAXC + 1)
    lengths = left * right // MAXC
    longest = jax.random.randint(third, (), 0, REQUESTS)
    return jnp.where(jnp.arange(REQUESTS) == longest, MAXC, lengths).astype(jnp.int32)


def draw_page_table(key, part):
    first, second = jax.random.split(key, 2)
    devices = MAXP // KPG
    request_keys = jax.random.split(first, REQUESTS)
    orders = jax.vmap(lambda one: jax.random.permutation(one, devices))(request_keys)
    numbers = jnp.arange(MAXP)
    home = orders[:, numbers % devices]
    device_keys = jax.random.split(second, devices)
    shuffles = jax.vmap(lambda one: jax.random.permutation(one, SLOTS))(device_keys)
    local = jnp.arange(REQUESTS)[:, None] * KPG + numbers[None, :] // devices
    slot = shuffles[home, local]
    return (home * SLOTS + slot).astype(jnp.int32)


def levels(stream_key, shape, cuts, low, high):
    factor_of = 1.0
    for dim, parts in cuts:
        draws = jax.random.uniform(jax.random.fold_in(jax.random.fold_in(stream_key, 6), dim), (parts,), jnp.float32, low / len(cuts), high / len(cuts))
        factor_of = factor_of * jnp.repeat(jnp.exp(draws), shape[dim] // parts).reshape((-1,) + (1,) * (len(shape) - 1 - dim))
    return factor_of


def routed_block(rng, own, number, rows, count, top, bound, slope):
    ranking = jax.random.permutation(rng, count)
    crowded, ordinary = shares(count, rows * top, bound, slope, True), shares(count, rows * top, bound, slope, False)
    places = jnp.arange(count)

    def named(tallies, rotation):
        used = int((tallies > 0).sum())
        fixed = max(1, used // 4)
        passed = fixed + (places - fixed + rotation * (used - fixed)) % max(1, count - fixed)
        return jnp.zeros((count,), jnp.int32).at[ranking[jnp.where(places < fixed, places, passed)]].set(jnp.asarray(tallies, jnp.int32))

    tallies = jnp.where(number % 4 == 0, named(crowded, number // 4), named(ordinary, number - number // 4 - 1))
    mixed = jax.random.permutation(jax.random.fold_in(own, 3), count)
    donor, taker = mixed[0:count // 2 * 2:2], mixed[1:count // 2 * 2:2]
    room = jnp.minimum(tallies[donor] - 1, bound - tallies[taker]) // 2
    room = jnp.where((donor == ranking[0]) | (taker == ranking[0]) | (tallies[taker] == 0), 0, jnp.maximum(room, 0))
    passed = jax.random.randint(jax.random.fold_in(own, 4), (count // 2,), 0, 1 << 20) % (room + 1)
    tallies = tallies.at[donor].add(-passed).at[taker].add(passed)
    members = jnp.searchsorted(jnp.cumsum(tallies), jnp.arange(rows * top), side="right").astype(jnp.int32)
    table = members.reshape(top, rows).T
    table = table[jax.random.permutation(jax.random.fold_in(own, 1), rows)]
    rotation = jax.random.randint(jax.random.fold_in(own, 2), (rows, 1), 0, top)
    return jnp.take_along_axis(table, (jnp.arange(top)[None, :] + rotation) % top, axis=1)


def shares(count, total, reach, skew, full):
    portions = [(1 << 20) // math.isqrt(grade ** skew) + 1 for grade in range(1, count + 1)]
    largest = reach if full else min(reach, max(-(-total // count), total * portions[0] // sum(portions)))
    least = 1 if total - largest >= count - 1 else 0
    counts, surplus = [largest] + [least] * (count - 1), total - largest - least * (count - 1)
    while surplus > 0:
        free = [i for i in range(1, count) if counts[i] < largest] or [i for i in range(1, count) if counts[i] < reach]
        mass, budget = sum([portions[i] for i in free]), surplus
        for i in free:
            addition = min(reach - counts[i], max(1, budget * portions[i] // mass), surplus)
            counts[i] = counts[i] + addition
            surplus = surplus - addition
    return np.array(counts)


def bell_draw(rng, dims, scale, bound, cuts=(), kind=jnp.bfloat16):
    entries = jax.random.normal(rng, dims, jnp.float32) * scale
    if len(cuts) > 0:
        entries = levels(rng, dims, cuts, -0.22, 0.18) * entries
    return jnp.clip(entries, min=-bound, max=bound).astype(kind)


def setup_inputs(seed: int = 0) -> dict:
    seeds = jax.random.split(jax.random.key(seed), 15)
    x_resid = bell_draw(seeds[0], (TOKENS, D), 1.0, 6.0, ((0, 32), (1, 8)))
    q_new = draw_q_new(jax.random.fold_in(seeds[14], 71), 0)
    kv_new = bell_draw(seeds[2], (TOKENS, KVH, 2 * HEAD), 1.0, 4.0, ((0, 32), (1, 8)))
    kv_cache = draw_kv_cache(jax.random.fold_in(seeds[14], 71), 0)
    cache_len = draw_cache_len(jax.random.fold_in(seeds[14], 71), 0)
    page_table = draw_page_table(jax.random.fold_in(seeds[14], 71), 0)
    sinks = jnp.clip(8.0 * jax.random.uniform(seeds[6], (QH,), jnp.float32) ** levels(seeds[6], (QH,), ((0, 8),), -0.2, 0.2), 0.0, 8.0)
    out_weight = bell_draw(seeds[7], (QH * HEAD, D), (QH * HEAD) ** -0.5, 0.09375, ((0, 8),))
    norm_gain = jnp.clip(1.0 + 0.18 * jax.random.normal(seeds[8], (D,), jnp.float32), 0.1, 1.9)
    routes_keys = jax.random.split(jax.random.fold_in(seeds[9], 1), TOKENS // TOK_DEV)
    routes_turns = jax.random.permutation(jax.random.fold_in(seeds[9], 3), TOKENS // TOK_DEV)
    routes = jax.vmap(lambda own, number: routed_block(jax.random.fold_in(seeds[9], 2), own, number, TOK_DEV, EXPERTS, TOPK, CAP, 2))(routes_keys, routes_turns).reshape((TOKENS, TOPK))
    route_wt = jnp.clip(0.05 + 0.45 * jax.random.uniform(seeds[10], (TOKENS, TOPK), jnp.float32) ** levels(seeds[10], (TOKENS, TOPK), ((0, 32),), -0.2, 0.2), 0.05, 0.5)
    w_gate = bell_draw(seeds[11], (EXPERTS, D, EF), D ** -0.5, 0.109375, ((0, 32), (2, 8)))
    w_up = bell_draw(seeds[12], (EXPERTS, D, EF), D ** -0.5, 0.109375, ((0, 32), (2, 8)))
    w_down = bell_draw(seeds[13], (EXPERTS, EF, D), EF ** -0.5, 0.109375, ((0, 32), (1, 8)))
    return {"x_resid": x_resid, "q_new": q_new, "kv_new": kv_new, "kv_cache": kv_cache, "cache_len": cache_len, "page_table": page_table, "sinks": sinks, "out_weight": out_weight, "norm_gain": norm_gain, "routes": routes, "route_wt": route_wt, "w_gate": w_gate, "w_up": w_up, "w_down": w_down}


rope_base = 150000.0
neg_big = -1e+30
norm_eps = 1e-05

def rotate(values, where):
    half = values.shape[-1] // 2
    freq = rope_base ** (-jnp.arange(half, dtype=jnp.float32) * 2.0 / values.shape[-1])
    angle = where.astype(jnp.float32)[:, None] * freq[None, :]
    cosine = jnp.cos(angle)[:, None, :]
    sine = jnp.sin(angle)[:, None, :]
    first = values[..., :half]
    second = values[..., half:]
    return jnp.concatenate([first * cosine - second * sine, first * sine + second * cosine], -1)

def reference(x_resid, q_new, kv_new, kv_cache, cache_len, page_table, sinks, out_weight, norm_gain, routes, route_wt, w_gate, w_up, w_down):

    def one_request(request):
        length = cache_len[request]
        where = length + jnp.arange(NEW, dtype=jnp.int32)
        q_rows = lax.dynamic_slice_in_dim(q_new, request * NEW, NEW, 0).reshape(NEW, QH, HEAD)
        queries = rotate(q_rows.astype(jnp.float32), where).astype(jnp.bfloat16)
        kv_rows = lax.dynamic_slice_in_dim(kv_new, request * NEW, NEW, 0)
        new_keys = rotate(kv_rows[..., :HEAD].astype(jnp.float32), where).astype(jnp.bfloat16)
        pages = kv_cache[page_table[request]].reshape(MAXC, KVH, 2 * HEAD)
        keys = jnp.concatenate([pages[..., :HEAD], new_keys], 0)
        values = jnp.concatenate([pages[..., HEAD:], kv_rows[..., HEAD:]], 0)
        token = jnp.arange(NEW, dtype=jnp.int32)[:, None]
        entry = jnp.arange(MAXC + NEW, dtype=jnp.int32)[None, :]
        allowed = jnp.where(entry < MAXC, entry < length, entry - MAXC <= token)

        def one_head(group_head):
            q_head = lax.dynamic_slice_in_dim(queries, group_head * QPK, QPK, 1).astype(jnp.float32)
            k_head = keys[:, group_head].astype(jnp.float32)
            v_head = values[:, group_head].astype(jnp.float32)
            scores = jnp.einsum('ngd,kd->gnk', q_head, k_head) * HEAD ** (-0.5)
            scores = jnp.where(allowed[None], scores, neg_big)
            sink = lax.dynamic_slice_in_dim(sinks, group_head * QPK, QPK)[:, None]
            top = jnp.maximum(lax.optimization_barrier(jnp.max(scores, -1)), sink)
            expo = jnp.exp(scores - top[..., None])
            weights = lax.optimization_barrier(expo.astype(jnp.bfloat16)).astype(jnp.float32)
            total = lax.optimization_barrier(jnp.sum(expo, -1)) + jnp.exp(sink - top)
            result = jnp.einsum('gnk,kd->gnd', weights, v_head) / total[..., None]
            return result.astype(jnp.bfloat16)
        heads = lax.map(one_head, jnp.arange(KVH, dtype=jnp.int32))
        return heads.transpose(2, 0, 1, 3).reshape(NEW, QH * HEAD)
    attended = lax.map(one_request, jnp.arange(REQUESTS, dtype=jnp.int32)).reshape(TOKENS, QH * HEAD)
    resid = (x_resid.astype(jnp.float32) + jnp.dot(attended, out_weight, preferred_element_type=jnp.float32)).astype(jnp.bfloat16)
    resid_wide = resid.astype(jnp.float32)
    scale_rows = lax.rsqrt(lax.optimization_barrier(jnp.mean(resid_wide * resid_wide, -1, keepdims=True)) + norm_eps)
    normed = (resid_wide * scale_rows * norm_gain[None, :]).astype(jnp.bfloat16)
    flat = routes.reshape(N_SEQ, TOK_DEV * TOPK)
    onehot = (flat[..., None] == jnp.arange(EXPERTS, dtype=jnp.int32)).astype(jnp.int32)
    running = (jnp.cumsum(onehot, 1) - 1).astype(jnp.int32)
    rank = lax.optimization_barrier(jnp.sum(onehot * running, -1)).astype(jnp.int32)
    block = jnp.broadcast_to(jnp.arange(N_SEQ, dtype=jnp.int32)[:, None], flat.shape)
    token_of = block * TOK_DEV + jnp.broadcast_to(jnp.arange(TOK_DEV * TOPK, dtype=jnp.int32)[None, :] // TOPK, flat.shape)
    source = jnp.full((EXPERTS, N_SEQ, CAP), TOKENS, jnp.int32).at[flat, block, rank].set(token_of.astype(jnp.int32))
    padded = jnp.concatenate([normed, jnp.zeros((1, D), jnp.bfloat16)], 0)

    def one_expert(expert):
        rows_in = padded[source[expert].reshape(-1)]
        hidden = jnp.dot(rows_in, w_gate[expert], preferred_element_type=jnp.float32)
        lin = jnp.dot(rows_in, w_up[expert], preferred_element_type=jnp.float32)
        act = (hidden * jax.nn.sigmoid(1.702 * hidden) * (lin + 1.0)).astype(jnp.bfloat16)
        pieces = jnp.einsum('rjf,jfd->jrd', act.reshape(N_SEQ * CAP, N_TP, EF // N_TP).astype(jnp.float32), w_down[expert].reshape(N_TP, EF // N_TP, D).astype(jnp.float32))
        pieces = lax.optimization_barrier(pieces.astype(jnp.bfloat16)).astype(jnp.float32)
        return lax.optimization_barrier(jnp.sum(pieces, 0)).astype(jnp.bfloat16)
    expert_out = lax.map(one_expert, jnp.arange(EXPERTS, dtype=jnp.int32)).reshape(EXPERTS * N_SEQ * CAP, D)
    position = (flat * (N_SEQ * CAP) + block * CAP + rank).reshape(TOKENS, TOPK).astype(jnp.int32)
    taken = expert_out[position].astype(jnp.float32)
    mixture = lax.optimization_barrier(jnp.sum(route_wt[..., None] * taken, 1))
    output = (resid_wide + mixture).astype(jnp.bfloat16)
    return (attended, output)
```

```python
import jax
import jax.numpy as jnp
from jax import lax
from jax.sharding import PartitionSpec as P

D = 2880
NEW = 128


rope_base = 150000.0
neg_big = -1e30
norm_eps = 1e-05


def rotate(values, where):
    half = values.shape[-1] // 2
    freq = rope_base ** (-jnp.arange(half, dtype=jnp.float32) * 2.0 / values.shape[-1])
    angle = where.astype(jnp.float32)[:, None] * freq[None, :]
    cosine = jnp.cos(angle)[:, None, :]
    sine = jnp.sin(angle)[:, None, :]
    first = values[..., :half]
    second = values[..., half:]
    return jnp.concatenate([first * cosine - second * sine, first * sine + second * cosine], -1)


def per_device(
    x_resid,
    q_new,
    kv_new,
    kv_cache,
    cache_len,
    page_table,
    sinks,
    out_weight,
    norm_gain,
    routes,
    route_wt,
    w_gate,
    w_up,
    w_down,
):
    seq_count = lax.axis_size("seq")
    seq_here = lax.axis_index("seq")
    rows, cols = x_resid.shape
    local_kv = kv_new.shape[1]
    head = kv_new.shape[2] // 2
    local_q = q_new.shape[1] // head
    group = local_q // local_kv
    slots = kv_cache.shape[0]
    page = kv_cache.shape[1]
    requests, max_pages = page_table.shape
    topk = routes.shape[1]
    assert rows == NEW and requests == seq_count and max_pages == seq_count

    length = cache_len[seq_here]
    where = length + jnp.arange(rows, dtype=jnp.int32)
    queries = rotate(q_new.reshape(rows, local_q, head).astype(jnp.float32), where).astype(
        jnp.bfloat16
    )
    fresh_keys = rotate(kv_new[..., :head].astype(jnp.float32), where).astype(jnp.bfloat16)
    fresh_vals = kv_new[..., head:]

    home = page_table // slots
    mine = home == seq_here
    slot_of = jnp.sum(jnp.where(mine, page_table % slots, 0), 1)
    outgoing = kv_cache[slot_of]
    incoming = lax.all_to_all(outgoing, "seq", split_axis=0, concat_axis=0, tiled=True)
    own_home = home[seq_here]
    page_ids = jnp.arange(max_pages, dtype=jnp.int32)
    src_ids = jnp.arange(seq_count, dtype=jnp.int32)
    page_of_src = jnp.sum(
        jnp.where(own_home[None, :] == src_ids[:, None], page_ids[None, :], 0), 1
    )
    spots = page_of_src[:, None] * page + jnp.arange(page, dtype=jnp.int32)[None, :]
    cache_ok = (spots < length).reshape(seq_count * page)
    cache_keys = incoming[..., :head].reshape(seq_count * page, local_kv, head)
    cache_vals = incoming[..., head:].reshape(seq_count * page, local_kv, head)

    q_g = queries.reshape(rows, local_kv, group, head)
    scale = head ** (-0.5)
    s_cache = jnp.einsum(
        "ngqd,kgd->gqnk", q_g, cache_keys, preferred_element_type=jnp.float32
    ) * scale
    s_cache = jnp.where(cache_ok[None, None, None, :], s_cache, neg_big)
    s_new = jnp.einsum(
        "ngqd,kgd->gqnk", q_g, fresh_keys, preferred_element_type=jnp.float32
    ) * scale
    tok = jnp.arange(rows, dtype=jnp.int32)
    causal = tok[None, :] <= tok[:, None]
    s_new = jnp.where(causal[None, None], s_new, neg_big)
    sink = sinks.reshape(local_kv, group)[:, :, None]
    top = jnp.maximum(jnp.maximum(jnp.max(s_cache, -1), jnp.max(s_new, -1)), sink)
    e_cache = jnp.exp(s_cache - top[..., None])
    e_new = jnp.exp(s_new - top[..., None])
    total = jnp.sum(e_cache, -1) + jnp.sum(e_new, -1) + jnp.exp(sink - top)
    summed = jnp.einsum(
        "gqnk,kgd->gqnd", e_cache.astype(jnp.bfloat16), cache_vals,
        preferred_element_type=jnp.float32,
    ) + jnp.einsum(
        "gqnk,kgd->gqnd", e_new.astype(jnp.bfloat16), fresh_vals,
        preferred_element_type=jnp.float32,
    )
    attended = (summed / total[..., None]).astype(jnp.bfloat16)
    attended = attended.transpose(2, 0, 1, 3).reshape(rows, local_q * head)

    partial_value = jnp.dot(attended, out_weight, preferred_element_type=jnp.float32)
    column_sums = lax.psum_scatter(
        partial_value.astype(jnp.bfloat16), "tp", scatter_dimension=1, tiled=True
    ).astype(jnp.float32)
    resid = (x_resid.astype(jnp.float32) + column_sums).astype(jnp.bfloat16)
    resid_wide = resid.astype(jnp.float32)
    resid_full = lax.all_gather(resid, "tp", axis=1, tiled=True).astype(jnp.float32)
    squares = jnp.sum(resid_full * resid_full, 1)
    scale_rows = lax.rsqrt(squares / D + norm_eps)
    normed_full = (resid_full * scale_rows[:, None] * norm_gain[None, :]).astype(jnp.bfloat16)

    local_e = w_gate.shape[0]
    experts_all = local_e * seq_count
    cap = 2 * rows * topk // experts_all
    flat_routes = routes.reshape(-1)
    onehot = (flat_routes[:, None] == jnp.arange(experts_all, dtype=jnp.int32)[None, :]).astype(
        jnp.int32
    )
    rank = jnp.sum(onehot * (jnp.cumsum(onehot, 0) - 1), 1)
    slot = flat_routes * cap + rank
    source = (
        jnp.full((experts_all * cap,), rows, jnp.int32)
        .at[slot]
        .set(jnp.arange(rows * topk, dtype=jnp.int32) // topk)
    )
    padded = jnp.concatenate([normed_full, jnp.zeros((1, D), jnp.bfloat16)], 0)
    outgoing_rows = padded[source].reshape(seq_count, local_e * cap, D)
    incoming_rows = lax.all_to_all(outgoing_rows, "seq", split_axis=0, concat_axis=0, tiled=True)
    arrived = incoming_rows.reshape(seq_count, local_e, cap, D)
    hidden = jnp.einsum("sexd,edf->sexf", arrived, w_gate, preferred_element_type=jnp.float32)
    lin = jnp.einsum("sexd,edf->sexf", arrived, w_up, preferred_element_type=jnp.float32)
    act = (hidden * jax.nn.sigmoid(1.702 * hidden) * (lin + 1.0)).astype(jnp.bfloat16)
    down = jnp.einsum("sexf,efd->sexd", act, w_down, preferred_element_type=jnp.float32)
    expert_out = lax.psum_scatter(down.astype(jnp.bfloat16), "tp", scatter_dimension=3, tiled=True)
    returned = lax.all_to_all(
        expert_out.reshape(seq_count, local_e * cap, cols),
        "seq",
        split_axis=0,
        concat_axis=0,
        tiled=True,
    )
    taken = (
        returned.reshape(experts_all * cap, cols)[slot]
        .reshape(rows, topk, cols)
        .astype(jnp.float32)
    )
    mixture = jnp.sum(route_wt[..., None] * taken, 1)
    output = (resid_wide + mixture).astype(jnp.bfloat16)
    return (attended, output)


def solution(mesh):
    in_specs = (
        P("seq", "tp"),
        P("seq", "tp"),
        P("seq", "tp", None),
        P("seq", None, "tp", None),
        P(),
        P(),
        P("tp"),
        P("tp", None),
        P(),
        P("seq", None),
        P("seq", None),
        P("seq", None, "tp"),
        P("seq", None, "tp"),
        P("seq", "tp", None),
    )
    out_specs = (P("seq", "tp"), P("seq", "tp"))
    return jax.shard_map(
        per_device, mesh=mesh, in_specs=in_specs, out_specs=out_specs, check_vma=False
    )
```

```python
import jax
import jax.numpy as jnp
from jax import lax
from jax.sharding import PartitionSpec as P

D = 2880
NEW = 128


rope_base = 150000.0
neg_big = -1e30
norm_eps = 1e-05


def rotate(values, where):
    half = values.shape[-1] // 2
    freq = rope_base ** (-jnp.arange(half, dtype=jnp.float32) * 2.0 / values.shape[-1])
    angle = where.astype(jnp.float32)[:, None] * freq[None, :]
    cosine = jnp.cos(angle)[:, None, :]
    sine = jnp.sin(angle)[:, None, :]
    first = values[..., :half]
    second = values[..., half:]
    return jnp.concatenate([first * cosine - second * sine, first * sine + second * cosine], -1)


def per_device(
    x_resid,
    q_new,
    kv_new,
    kv_cache,
    cache_len,
    page_table,
    sinks,
    out_weight,
    norm_gain,
    routes,
    route_wt,
    w_gate,
    w_up,
    w_down,
):
    seq_count = lax.axis_size("seq")
    seq_here = lax.axis_index("seq")
    rows, cols = x_resid.shape
    local_kv = kv_new.shape[1]
    head = kv_new.shape[2] // 2
    local_q = q_new.shape[1] // head
    group = local_q // local_kv
    slots = kv_cache.shape[0]
    page = kv_cache.shape[1]
    requests, max_pages = page_table.shape
    topk = routes.shape[1]
    assert rows == NEW and requests == seq_count and max_pages == seq_count

    length = cache_len[seq_here]
    where = length + jnp.arange(rows, dtype=jnp.int32)
    queries = rotate(q_new.reshape(rows, local_q, head).astype(jnp.float32), where).astype(
        jnp.bfloat16
    )
    fresh_keys = rotate(kv_new[..., :head].astype(jnp.float32), where).astype(jnp.bfloat16)
    fresh_vals = kv_new[..., head:]

    home = page_table // slots
    mine = home == seq_here
    slot_of = jnp.sum(jnp.where(mine, page_table % slots, 0), 1)
    outgoing = kv_cache[slot_of]
    incoming = lax.all_to_all(outgoing, "seq", split_axis=0, concat_axis=0, tiled=True)
    own_home = home[seq_here]
    page_ids = jnp.arange(max_pages, dtype=jnp.int32)
    src_ids = jnp.arange(seq_count, dtype=jnp.int32)
    page_of_src = jnp.sum(
        jnp.where(own_home[None, :] == src_ids[:, None], page_ids[None, :], 0), 1
    )
    spots = page_of_src[:, None] * page + jnp.arange(page, dtype=jnp.int32)[None, :]
    cache_ok = (spots < length).reshape(seq_count * page)
    cache_keys = incoming[..., :head].reshape(seq_count * page, local_kv, head)
    cache_vals = incoming[..., head:].reshape(seq_count * page, local_kv, head)

    q_g = queries.reshape(rows, local_kv, group, head)
    scale = head ** (-0.5)
    s_cache = jnp.einsum(
        "ngqd,kgd->gqnk", q_g, cache_keys, preferred_element_type=jnp.float32
    ) * scale
    s_cache = jnp.where(cache_ok[None, None, None, :], s_cache, neg_big)
    s_new = jnp.einsum(
        "ngqd,kgd->gqnk", q_g, fresh_keys, preferred_element_type=jnp.float32
    ) * scale
    tok = jnp.arange(rows, dtype=jnp.int32)
    causal = tok[None, :] <= tok[:, None]
    s_new = jnp.where(causal[None, None], s_new, neg_big)
    sink = sinks.reshape(local_kv, group)[:, :, None]
    top = jnp.maximum(jnp.maximum(jnp.max(s_cache, -1), jnp.max(s_new, -1)), sink)
    e_cache = jnp.exp(s_cache - top[..., None])
    e_new = jnp.exp(s_new - top[..., None])
    total = jnp.sum(e_cache, -1) + jnp.sum(e_new, -1) + jnp.exp(sink - top)
    summed = jnp.einsum(
        "gqnk,kgd->gqnd", e_cache.astype(jnp.bfloat16), cache_vals,
        preferred_element_type=jnp.float32,
    ) + jnp.einsum(
        "gqnk,kgd->gqnd", e_new.astype(jnp.bfloat16), fresh_vals,
        preferred_element_type=jnp.float32,
    )
    attended = (summed / total[..., None]).astype(jnp.bfloat16)
    attended = attended.transpose(2, 0, 1, 3).reshape(rows, local_q * head)

    partial_value = jnp.dot(attended, out_weight, preferred_element_type=jnp.float32)
    column_sums = lax.psum_scatter(
        partial_value.astype(jnp.bfloat16), "tp", scatter_dimension=1, tiled=True
    ).astype(jnp.float32)
    resid = (x_resid.astype(jnp.float32) + column_sums).astype(jnp.bfloat16)
    resid_wide = resid.astype(jnp.float32)
    resid_full = lax.all_gather(resid, "tp", axis=1, tiled=True).astype(jnp.float32)
    squares = jnp.sum(resid_full * resid_full, 1)
    scale_rows = lax.rsqrt(squares / D + norm_eps)
    normed_full = (resid_full * scale_rows[:, None] * norm_gain[None, :]).astype(jnp.bfloat16)

    local_e = w_gate.shape[0]
    experts_all = local_e * seq_count
    cap = 2 * rows * topk // experts_all
    flat_routes = routes.reshape(-1)
    onehot = (flat_routes[:, None] == jnp.arange(experts_all, dtype=jnp.int32)[None, :]).astype(
        jnp.int32
    )
    rank = jnp.sum(onehot * (jnp.cumsum(onehot, 0) - 1), 1)
    slot = flat_routes * cap + rank
    source = (
        jnp.full((experts_all * cap,), rows, jnp.int32)
        .at[slot]
        .set(jnp.arange(rows * topk, dtype=jnp.int32) // topk)
    )
    padded = jnp.concatenate([normed_full, jnp.zeros((1, D), jnp.bfloat16)], 0)
    outgoing_rows = padded[source].reshape(seq_count, local_e * cap, D)
    incoming_rows = lax.all_to_all(outgoing_rows, "seq", split_axis=0, concat_axis=0, tiled=True)
    arrived = incoming_rows.reshape(seq_count, local_e, cap, D)
    hidden = jnp.einsum("sexd,edf->sexf", arrived, w_gate, preferred_element_type=jnp.float32)
    lin = jnp.einsum("sexd,edf->sexf", arrived, w_up, preferred_element_type=jnp.float32)
    act = (hidden * jax.nn.sigmoid(1.702 * hidden) * (lin + 1.0)).astype(jnp.bfloat16)
    tp_count = D // cols
    w_down_split = w_down.reshape(local_e, w_down.shape[1], tp_count, cols)
    down = jnp.einsum(
        "sexf,efjk->jsexk", act, w_down_split, preferred_element_type=jnp.float32
    ).astype(jnp.bfloat16)
    down = down.reshape(tp_count * seq_count * local_e * cap, cols)
    expert_out = lax.psum_scatter(down, "tp", scatter_dimension=0, tiled=True)
    returned = lax.all_to_all(
        expert_out.reshape(seq_count, local_e * cap, cols),
        "seq",
        split_axis=0,
        concat_axis=0,
        tiled=True,
    )
    taken = (
        returned.reshape(experts_all * cap, cols)[slot]
        .reshape(rows, topk, cols)
        .astype(jnp.float32)
    )
    mixture = jnp.sum(route_wt[..., None] * taken, 1)
    output = (resid_wide + mixture).astype(jnp.bfloat16)
    return (attended, output)


def solution(mesh):
    in_specs = (
        P("seq", "tp"),
        P("seq", "tp"),
        P("seq", "tp", None),
        P("seq", None, "tp", None),
        P(),
        P(),
        P("tp"),
        P("tp", None),
        P(),
        P("seq", None),
        P("seq", None),
        P("seq", None, "tp"),
        P("seq", None, "tp"),
        P("seq", "tp", None),
    )
    out_specs = (P("seq", "tp"), P("seq", "tp"))
    return jax.shard_map(
        per_device, mesh=mesh, in_specs=in_specs, out_specs=out_specs, check_vma=False
    )
```

```python
import jax
import jax.numpy as jnp
from jax import lax
from jax.sharding import PartitionSpec as P

D = 2880
NEW = 128


rope_base = 150000.0
neg_big = -1e30
norm_eps = 1e-05


def rotate(values, where):
    half = values.shape[-1] // 2
    freq = rope_base ** (-jnp.arange(half, dtype=jnp.float32) * 2.0 / values.shape[-1])
    angle = where.astype(jnp.float32)[:, None] * freq[None, :]
    cosine = jnp.cos(angle)[:, None, :]
    sine = jnp.sin(angle)[:, None, :]
    first = values[..., :half]
    second = values[..., half:]
    return jnp.concatenate([first * cosine - second * sine, first * sine + second * cosine], -1)


def per_device(
    x_resid,
    q_new,
    kv_new,
    kv_cache,
    cache_len,
    page_table,
    sinks,
    out_weight,
    norm_gain,
    routes,
    route_wt,
    w_gate,
    w_up,
    w_down,
):
    seq_count = lax.axis_size("seq")
    seq_here = lax.axis_index("seq")
    rows, cols = x_resid.shape
    local_kv = kv_new.shape[1]
    head = kv_new.shape[2] // 2
    local_q = q_new.shape[1] // head
    group = local_q // local_kv
    slots = kv_cache.shape[0]
    page = kv_cache.shape[1]
    requests, max_pages = page_table.shape
    topk = routes.shape[1]
    assert rows == NEW and requests == seq_count and max_pages == seq_count

    length = cache_len[seq_here]
    where = length + jnp.arange(rows, dtype=jnp.int32)
    queries = rotate(q_new.reshape(rows, local_q, head).astype(jnp.float32), where).astype(
        jnp.bfloat16
    )
    fresh_keys = rotate(kv_new[..., :head].astype(jnp.float32), where).astype(jnp.bfloat16)
    fresh_vals = kv_new[..., head:]

    home = page_table // slots
    mine = home == seq_here
    slot_of = jnp.sum(jnp.where(mine, page_table % slots, 0), 1)
    outgoing = kv_cache[slot_of]
    incoming = lax.all_to_all(outgoing, "seq", split_axis=0, concat_axis=0, tiled=True)
    own_home = home[seq_here]
    page_ids = jnp.arange(max_pages, dtype=jnp.int32)
    src_ids = jnp.arange(seq_count, dtype=jnp.int32)
    page_of_src = jnp.sum(
        jnp.where(own_home[None, :] == src_ids[:, None], page_ids[None, :], 0), 1
    )
    spots = page_of_src[:, None] * page + jnp.arange(page, dtype=jnp.int32)[None, :]
    cache_ok = (spots < length).reshape(seq_count * page)
    cache_keys = incoming[..., :head].reshape(seq_count * page, local_kv, head)
    cache_vals = incoming[..., head:].reshape(seq_count * page, local_kv, head)

    q_g = queries.reshape(rows, local_kv, group, head)
    scale = head ** (-0.5)
    s_cache = jnp.einsum(
        "ngqd,kgd->gqnk", q_g, cache_keys, preferred_element_type=jnp.float32
    ) * scale
    s_cache = jnp.where(cache_ok[None, None, None, :], s_cache, neg_big)
    s_new = jnp.einsum(
        "ngqd,kgd->gqnk", q_g, fresh_keys, preferred_element_type=jnp.float32
    ) * scale
    tok = jnp.arange(rows, dtype=jnp.int32)
    causal = tok[None, :] <= tok[:, None]
    s_new = jnp.where(causal[None, None], s_new, neg_big)
    sink = sinks.reshape(local_kv, group)[:, :, None]
    top = jnp.maximum(jnp.maximum(jnp.max(s_cache, -1), jnp.max(s_new, -1)), sink)
    e_cache = jnp.exp(s_cache - top[..., None])
    e_new = jnp.exp(s_new - top[..., None])
    total = jnp.sum(e_cache, -1) + jnp.sum(e_new, -1) + jnp.exp(sink - top)
    summed = jnp.einsum(
        "gqnk,kgd->gqnd", e_cache.astype(jnp.bfloat16), cache_vals,
        preferred_element_type=jnp.float32,
    ) + jnp.einsum(
        "gqnk,kgd->gqnd", e_new.astype(jnp.bfloat16), fresh_vals,
        preferred_element_type=jnp.float32,
    )
    attended = (summed / total[..., None]).astype(jnp.bfloat16)
    attended = attended.transpose(2, 0, 1, 3).reshape(rows, local_q * head)

    partial_value = jnp.dot(attended, out_weight, preferred_element_type=jnp.float32)
    tp_count = D // cols
    blocks = partial_value.astype(jnp.bfloat16).reshape(rows, tp_count, cols).transpose(1, 0, 2)
    blocks = lax.all_to_all(blocks, "tp", split_axis=0, concat_axis=0, tiled=True)
    column_sums = jnp.sum(blocks.astype(jnp.float32), 0)
    resid = (x_resid.astype(jnp.float32) + column_sums).astype(jnp.bfloat16)
    resid_wide = resid.astype(jnp.float32)
    spread = jnp.broadcast_to(resid[None], (tp_count, rows, cols))
    spread = lax.all_to_all(spread, "tp", split_axis=0, concat_axis=0, tiled=True)
    resid_full = spread.transpose(1, 0, 2).reshape(rows, D).astype(jnp.float32)
    squares = jnp.sum(resid_full * resid_full, 1)
    scale_rows = lax.rsqrt(squares / D + norm_eps)
    normed_full = (resid_full * scale_rows[:, None] * norm_gain[None, :]).astype(jnp.bfloat16)

    local_e = w_gate.shape[0]
    experts_all = local_e * seq_count
    cap = 2 * rows * topk // experts_all
    flat_routes = routes.reshape(-1)
    onehot = (flat_routes[:, None] == jnp.arange(experts_all, dtype=jnp.int32)[None, :]).astype(
        jnp.int32
    )
    rank = jnp.sum(onehot * (jnp.cumsum(onehot, 0) - 1), 1)
    slot = flat_routes * cap + rank
    source = (
        jnp.full((experts_all * cap,), rows, jnp.int32)
        .at[slot]
        .set(jnp.arange(rows * topk, dtype=jnp.int32) // topk)
    )
    picks = (source[:, None] == jnp.arange(rows, dtype=jnp.int32)[None, :]).astype(jnp.bfloat16)
    outgoing_rows = jnp.dot(picks, normed_full, preferred_element_type=jnp.float32).astype(
        jnp.bfloat16
    ).reshape(seq_count, local_e, cap, D)
    w_down_split = w_down.reshape(local_e, w_down.shape[1], tp_count, cols)
    chunks = 2
    part = cap // chunks
    pieces = []
    for c in range(chunks):
        sent = outgoing_rows[:, :, c * part:(c + 1) * part].reshape(seq_count, local_e * part, D)
        arrived = lax.all_to_all(sent, "seq", split_axis=0, concat_axis=0, tiled=True)
        arrived = arrived.reshape(seq_count, local_e, part, D)
        hidden = jnp.einsum("sexd,edf->sexf", arrived, w_gate, preferred_element_type=jnp.float32)
        lin = jnp.einsum("sexd,edf->sexf", arrived, w_up, preferred_element_type=jnp.float32)
        act = (hidden * jax.nn.sigmoid(1.702 * hidden) * (lin + 1.0)).astype(jnp.bfloat16)
        down = jnp.einsum(
            "sexf,efjk->jsexk", act, w_down_split, preferred_element_type=jnp.float32
        ).astype(jnp.bfloat16)
        down = down.reshape(tp_count * seq_count * local_e * part, cols)
        expert_out = lax.psum_scatter(down, "tp", scatter_dimension=0, tiled=True)
        back = lax.all_to_all(
            expert_out.reshape(seq_count, local_e * part, cols),
            "seq",
            split_axis=0,
            concat_axis=0,
            tiled=True,
        )
        pieces.append(back.reshape(seq_count, local_e, part, cols))
    returned = jnp.concatenate(pieces, 2)
    taken = (
        returned.reshape(experts_all * cap, cols)[slot]
        .reshape(rows, topk, cols)
        .astype(jnp.float32)
    )
    mixture = jnp.sum(route_wt[..., None] * taken, 1)
    output = (resid_wide + mixture).astype(jnp.bfloat16)
    return (attended, output)


def solution(mesh):
    in_specs = (
        P("seq", "tp"),
        P("seq", "tp"),
        P("seq", "tp", None),
        P("seq", None, "tp", None),
        P(),
        P(),
        P("tp"),
        P("tp", None),
        P(),
        P("seq", None),
        P("seq", None),
        P("seq", None, "tp"),
        P("seq", None, "tp"),
        P("seq", "tp", None),
    )
    out_specs = (P("seq", "tp"), P("seq", "tp"))
    return jax.shard_map(
        per_device, mesh=mesh, in_specs=in_specs, out_specs=out_specs, check_vma=False
    )
```

```python
import jax
import jax.numpy as jnp
from jax import lax
from jax.sharding import PartitionSpec as P

D = 2880
NEW = 128


rope_base = 150000.0
neg_big = -1e30
norm_eps = 1e-05


def rotate(values, where):
    half = values.shape[-1] // 2
    freq = rope_base ** (-jnp.arange(half, dtype=jnp.float32) * 2.0 / values.shape[-1])
    angle = where.astype(jnp.float32)[:, None] * freq[None, :]
    cosine = jnp.cos(angle)[:, None, :]
    sine = jnp.sin(angle)[:, None, :]
    first = values[..., :half]
    second = values[..., half:]
    return jnp.concatenate([first * cosine - second * sine, first * sine + second * cosine], -1)


def per_device(
    x_resid,
    q_new,
    kv_new,
    kv_cache,
    cache_len,
    page_table,
    sinks,
    out_weight,
    norm_gain,
    routes,
    route_wt,
    w_gate,
    w_up,
    w_down,
):
    seq_count = lax.axis_size("seq")
    seq_here = lax.axis_index("seq")
    rows, cols = x_resid.shape
    local_kv = kv_new.shape[1]
    head = kv_new.shape[2] // 2
    local_q = q_new.shape[1] // head
    group = local_q // local_kv
    slots = kv_cache.shape[0]
    page = kv_cache.shape[1]
    requests, max_pages = page_table.shape
    topk = routes.shape[1]
    assert rows == NEW and requests == seq_count and max_pages == seq_count

    length = cache_len[seq_here]
    where = length + jnp.arange(rows, dtype=jnp.int32)
    queries = rotate(q_new.reshape(rows, local_q, head).astype(jnp.float32), where).astype(
        jnp.bfloat16
    )
    fresh_keys = rotate(kv_new[..., :head].astype(jnp.float32), where).astype(jnp.bfloat16)
    fresh_vals = kv_new[..., head:]

    home = page_table // slots
    mine = home == seq_here
    slot_of = jnp.sum(jnp.where(mine, page_table % slots, 0), 1)
    outgoing = kv_cache[slot_of]
    incoming = lax.all_to_all(outgoing, "seq", split_axis=0, concat_axis=0, tiled=True)
    own_home = home[seq_here]
    page_ids = jnp.arange(max_pages, dtype=jnp.int32)
    src_ids = jnp.arange(seq_count, dtype=jnp.int32)
    page_of_src = jnp.sum(
        jnp.where(own_home[None, :] == src_ids[:, None], page_ids[None, :], 0), 1
    )
    spots = page_of_src[:, None] * page + jnp.arange(page, dtype=jnp.int32)[None, :]
    cache_ok = (spots < length).reshape(seq_count * page)
    cache_keys = incoming[..., :head].reshape(seq_count * page, local_kv, head)
    cache_vals = incoming[..., head:].reshape(seq_count * page, local_kv, head)

    q_g = queries.reshape(rows, local_kv, group, head)
    scale = head ** (-0.5)
    s_cache = jnp.einsum(
        "ngqd,kgd->gqnk", q_g, cache_keys, preferred_element_type=jnp.float32
    ) * scale
    s_cache = jnp.where(cache_ok[None, None, None, :], s_cache, neg_big)
    s_new = jnp.einsum(
        "ngqd,kgd->gqnk", q_g, fresh_keys, preferred_element_type=jnp.float32
    ) * scale
    tok = jnp.arange(rows, dtype=jnp.int32)
    causal = tok[None, :] <= tok[:, None]
    s_new = jnp.where(causal[None, None], s_new, neg_big)
    sink = sinks.reshape(local_kv, group)[:, :, None]
    top = jnp.maximum(jnp.maximum(jnp.max(s_cache, -1), jnp.max(s_new, -1)), sink)
    e_cache = jnp.exp(s_cache - top[..., None])
    e_new = jnp.exp(s_new - top[..., None])
    total = jnp.sum(e_cache, -1) + jnp.sum(e_new, -1) + jnp.exp(sink - top)
    summed = jnp.einsum(
        "gqnk,kgd->gqnd", e_cache.astype(jnp.bfloat16), cache_vals,
        preferred_element_type=jnp.float32,
    ) + jnp.einsum(
        "gqnk,kgd->gqnd", e_new.astype(jnp.bfloat16), fresh_vals,
        preferred_element_type=jnp.float32,
    )
    attended = (summed / total[..., None]).astype(jnp.bfloat16)
    attended = attended.transpose(2, 0, 1, 3).reshape(rows, local_q * head)

    partial_value = jnp.dot(attended, out_weight, preferred_element_type=jnp.float32)
    tp_count = D // cols
    blocks = partial_value.astype(jnp.bfloat16).reshape(rows, tp_count, cols).transpose(1, 0, 2)
    column_sums = lax.psum_scatter(
        blocks.reshape(tp_count * rows, cols), "tp", scatter_dimension=0, tiled=True
    ).astype(jnp.float32)
    resid = (x_resid.astype(jnp.float32) + column_sums).astype(jnp.bfloat16)
    resid_wide = resid.astype(jnp.float32)
    spread = jnp.broadcast_to(resid[None], (tp_count, rows, cols))
    spread = lax.all_to_all(spread, "tp", split_axis=0, concat_axis=0, tiled=True)
    resid_full = spread.transpose(1, 0, 2).reshape(rows, D).astype(jnp.float32)
    squares = jnp.sum(resid_full * resid_full, 1)
    scale_rows = lax.rsqrt(squares / D + norm_eps)
    normed_full = (resid_full * scale_rows[:, None] * norm_gain[None, :]).astype(jnp.bfloat16)

    local_e = w_gate.shape[0]
    experts_all = local_e * seq_count
    cap = 2 * rows * topk // experts_all
    flat_routes = routes.reshape(-1)
    onehot = (flat_routes[:, None] == jnp.arange(experts_all, dtype=jnp.int32)[None, :]).astype(
        jnp.int32
    )
    rank = jnp.sum(onehot * (jnp.cumsum(onehot, 0) - 1), 1)
    slot = flat_routes * cap + rank
    source = (
        jnp.full((experts_all * cap,), rows, jnp.int32)
        .at[slot]
        .set(jnp.arange(rows * topk, dtype=jnp.int32) // topk)
    )
    picks = (source[:, None] == jnp.arange(rows, dtype=jnp.int32)[None, :]).astype(jnp.bfloat16)
    outgoing_rows = jnp.dot(picks, normed_full, preferred_element_type=jnp.float32).astype(
        jnp.bfloat16
    ).reshape(seq_count, local_e, cap, D)
    w_down_split = w_down.reshape(local_e, w_down.shape[1], tp_count, cols)
    chunks = 2
    part = cap // chunks
    pieces = []
    for c in range(chunks):
        sent = outgoing_rows[:, :, c * part:(c + 1) * part].reshape(seq_count, local_e * part, D)
        arrived = lax.all_to_all(sent, "seq", split_axis=0, concat_axis=0, tiled=True)
        arrived = arrived.reshape(seq_count, local_e, part, D)
        hidden = jnp.einsum("sexd,edf->sexf", arrived, w_gate, preferred_element_type=jnp.float32)
        lin = jnp.einsum("sexd,edf->sexf", arrived, w_up, preferred_element_type=jnp.float32)
        act = (hidden * jax.nn.sigmoid(1.702 * hidden) * (lin + 1.0)).astype(jnp.bfloat16)
        down = jnp.einsum(
            "sexf,efjk->jsexk", act, w_down_split, preferred_element_type=jnp.float32
        ).astype(jnp.bfloat16)
        down = down.reshape(tp_count * seq_count * local_e * part, cols)
        expert_out = lax.psum_scatter(down, "tp", scatter_dimension=0, tiled=True)
        back = lax.all_to_all(
            expert_out.reshape(seq_count, local_e * part, cols),
            "seq",
            split_axis=0,
            concat_axis=0,
            tiled=True,
        )
        pieces.append(back.reshape(seq_count, local_e, part, cols))
    returned = jnp.concatenate(pieces, 2)
    taken = (
        returned.reshape(experts_all * cap, cols)[slot]
        .reshape(rows, topk, cols)
        .astype(jnp.float32)
    )
    mixture = jnp.sum(route_wt[..., None] * taken, 1)
    output = (resid_wide + mixture).astype(jnp.bfloat16)
    return (attended, output)


def solution(mesh):
    in_specs = (
        P("seq", "tp"),
        P("seq", "tp"),
        P("seq", "tp", None),
        P("seq", None, "tp", None),
        P(),
        P(),
        P("tp"),
        P("tp", None),
        P(),
        P("seq", None),
        P("seq", None),
        P("seq", None, "tp"),
        P("seq", None, "tp"),
        P("seq", "tp", None),
    )
    out_specs = (P("seq", "tp"), P("seq", "tp"))
    return jax.shard_map(
        per_device, mesh=mesh, in_specs=in_specs, out_specs=out_specs, check_vma=False
    )
```

```python
import jax
import jax.numpy as jnp
from jax import lax
from jax.experimental.layout import Layout, with_layout_constraint
from jax.sharding import PartitionSpec as P

D = 2880
NEW = 128


rope_base = 150000.0
neg_big = -1e30
norm_eps = 1e-05


def rotate(values, where):
    half = values.shape[-1] // 2
    freq = rope_base ** (-jnp.arange(half, dtype=jnp.float32) * 2.0 / values.shape[-1])
    angle = where.astype(jnp.float32)[:, None] * freq[None, :]
    cosine = jnp.cos(angle)[:, None, :]
    sine = jnp.sin(angle)[:, None, :]
    first = values[..., :half]
    second = values[..., half:]
    return jnp.concatenate([first * cosine - second * sine, first * sine + second * cosine], -1)


def per_device(
    x_resid,
    q_new,
    kv_new,
    kv_cache,
    cache_len,
    page_table,
    sinks,
    out_weight,
    norm_gain,
    routes,
    route_wt,
    w_gate,
    w_up,
    w_down,
):
    seq_count = lax.axis_size("seq")
    seq_here = lax.axis_index("seq")
    rows, cols = x_resid.shape
    local_kv = kv_new.shape[1]
    head = kv_new.shape[2] // 2
    local_q = q_new.shape[1] // head
    group = local_q // local_kv
    slots = kv_cache.shape[0]
    page = kv_cache.shape[1]
    requests, max_pages = page_table.shape
    topk = routes.shape[1]
    assert rows == NEW and requests == seq_count and max_pages == seq_count

    length = cache_len[seq_here]
    where = length + jnp.arange(rows, dtype=jnp.int32)
    queries = rotate(q_new.reshape(rows, local_q, head).astype(jnp.float32), where).astype(
        jnp.bfloat16
    )
    fresh_keys = rotate(kv_new[..., :head].astype(jnp.float32), where).astype(jnp.bfloat16)
    fresh_vals = kv_new[..., head:]

    home = page_table // slots
    mine = home == seq_here
    slot_of = jnp.sum(jnp.where(mine, page_table % slots, 0), 1)
    outgoing = kv_cache[slot_of]
    incoming = lax.all_to_all(outgoing, "seq", split_axis=0, concat_axis=0, tiled=True)
    own_home = home[seq_here]
    page_ids = jnp.arange(max_pages, dtype=jnp.int32)
    src_ids = jnp.arange(seq_count, dtype=jnp.int32)
    page_of_src = jnp.sum(
        jnp.where(own_home[None, :] == src_ids[:, None], page_ids[None, :], 0), 1
    )
    spots = page_of_src[:, None] * page + jnp.arange(page, dtype=jnp.int32)[None, :]
    cache_ok = (spots < length).reshape(seq_count * page)
    cache_keys = incoming[..., :head].reshape(seq_count * page, local_kv, head)
    cache_vals = incoming[..., head:].reshape(seq_count * page, local_kv, head)

    q_g = queries.reshape(rows, local_kv, group, head)
    scale = head ** (-0.5)
    s_cache = jnp.einsum(
        "ngqd,kgd->gqnk", q_g, cache_keys, preferred_element_type=jnp.float32
    ) * scale
    s_cache = jnp.where(cache_ok[None, None, None, :], s_cache, neg_big)
    s_new = jnp.einsum(
        "ngqd,kgd->gqnk", q_g, fresh_keys, preferred_element_type=jnp.float32
    ) * scale
    tok = jnp.arange(rows, dtype=jnp.int32)
    causal = tok[None, :] <= tok[:, None]
    s_new = jnp.where(causal[None, None], s_new, neg_big)
    sink = sinks.reshape(local_kv, group)[:, :, None]
    top = jnp.maximum(jnp.maximum(jnp.max(s_cache, -1), jnp.max(s_new, -1)), sink)
    e_cache = jnp.exp(s_cache - top[..., None])
    e_new = jnp.exp(s_new - top[..., None])
    total = jnp.sum(e_cache, -1) + jnp.sum(e_new, -1) + jnp.exp(sink - top)
    summed = jnp.einsum(
        "gqnk,kgd->gqnd", e_cache.astype(jnp.bfloat16), cache_vals,
        preferred_element_type=jnp.float32,
    ) + jnp.einsum(
        "gqnk,kgd->gqnd", e_new.astype(jnp.bfloat16), fresh_vals,
        preferred_element_type=jnp.float32,
    )
    attended = (summed / total[..., None]).astype(jnp.bfloat16)
    attended = attended.transpose(2, 0, 1, 3).reshape(rows, local_q * head)

    partial_value = jnp.dot(attended, out_weight, preferred_element_type=jnp.float32)
    tp_count = D // cols
    blocks = partial_value.astype(jnp.bfloat16).reshape(rows, tp_count, cols).transpose(1, 0, 2)
    blocks = lax.all_to_all(blocks, "tp", split_axis=0, concat_axis=0, tiled=True)
    column_sums = jnp.sum(blocks.astype(jnp.float32), 0)
    resid = (x_resid.astype(jnp.float32) + column_sums).astype(jnp.bfloat16)
    resid_wide = resid.astype(jnp.float32)
    spread = jnp.broadcast_to(resid[None], (tp_count, rows, cols))
    spread = lax.all_to_all(spread, "tp", split_axis=0, concat_axis=0, tiled=True)
    resid_full = spread.transpose(1, 0, 2).reshape(rows, D).astype(jnp.float32)
    squares = jnp.sum(resid_full * resid_full, 1)
    scale_rows = lax.rsqrt(squares / D + norm_eps)
    normed_full = (resid_full * scale_rows[:, None] * norm_gain[None, :]).astype(jnp.bfloat16)

    local_e = w_gate.shape[0]
    experts_all = local_e * seq_count
    cap = 2 * rows * topk // experts_all
    chunks = 2
    part = cap // chunks
    flat_routes = routes.reshape(-1)
    onehot = (flat_routes[:, None] == jnp.arange(experts_all, dtype=jnp.int32)[None, :]).astype(
        jnp.int32
    )
    rank = jnp.sum(onehot * (jnp.cumsum(onehot, 0) - 1), 1)
    slot = (rank // part) * (experts_all * part) + flat_routes * part + rank % part
    source = (
        jnp.full((experts_all * cap,), rows, jnp.int32)
        .at[slot]
        .set(jnp.arange(rows * topk, dtype=jnp.int32) // topk)
    ).reshape(chunks, experts_all * part)
    token_ids = jnp.arange(rows, dtype=jnp.int32)
    w_down_split = w_down.reshape(local_e, w_down.shape[1], tp_count, cols)
    row_major2 = Layout(major_to_minor=(0, 1))
    pieces = []
    for c in range(chunks):
        picks = (source[c][:, None] == token_ids[None, :]).astype(jnp.bfloat16)
        sent = jnp.dot(picks, normed_full, preferred_element_type=jnp.float32).astype(
            jnp.bfloat16
        )
        sent = with_layout_constraint(sent, row_major2).reshape(seq_count, local_e * part, D)
        arrived = lax.all_to_all(sent, "seq", split_axis=0, concat_axis=0, tiled=True)
        arrived = arrived.reshape(seq_count, local_e, part, D)
        hidden = jnp.einsum("sexd,edf->sexf", arrived, w_gate, preferred_element_type=jnp.float32)
        lin = jnp.einsum("sexd,edf->sexf", arrived, w_up, preferred_element_type=jnp.float32)
        act = (hidden * jax.nn.sigmoid(1.702 * hidden) * (lin + 1.0)).astype(jnp.bfloat16)
        down = jnp.einsum(
            "sexf,efjk->jsexk", act, w_down_split, preferred_element_type=jnp.float32
        ).astype(jnp.bfloat16)
        down = with_layout_constraint(down, Layout(major_to_minor=(0, 1, 2, 3, 4)))
        down = down.reshape(tp_count * seq_count * local_e * part, cols)
        expert_out = lax.psum_scatter(down, "tp", scatter_dimension=0, tiled=True)
        back = lax.all_to_all(
            expert_out.reshape(seq_count, local_e * part, cols),
            "seq",
            split_axis=0,
            concat_axis=0,
            tiled=True,
        )
        pieces.append(back)
    returned = jnp.stack(pieces, 0)
    taken = (
        returned.reshape(experts_all * cap, cols)[slot]
        .reshape(rows, topk, cols)
        .astype(jnp.float32)
    )
    mixture = jnp.sum(route_wt[..., None] * taken, 1)
    output = (resid_wide + mixture).astype(jnp.bfloat16)
    return (attended, output)


def solution(mesh):
    in_specs = (
        P("seq", "tp"),
        P("seq", "tp"),
        P("seq", "tp", None),
        P("seq", None, "tp", None),
        P(),
        P(),
        P("tp"),
        P("tp", None),
        P(),
        P("seq", None),
        P("seq", None),
        P("seq", None, "tp"),
        P("seq", None, "tp"),
        P("seq", "tp", None),
    )
    out_specs = (P("seq", "tp"), P("seq", "tp"))
    return jax.shard_map(
        per_device, mesh=mesh, in_specs=in_specs, out_specs=out_specs, check_vma=False
    )
```

```python
import jax
import jax.numpy as jnp
from jax import lax
from jax.experimental.layout import Layout, with_layout_constraint
from jax.sharding import PartitionSpec as P

D = 2880
NEW = 128


rope_base = 150000.0
neg_big = -1e30
norm_eps = 1e-05


def rotate(values, where):
    half = values.shape[-1] // 2
    freq = rope_base ** (-jnp.arange(half, dtype=jnp.float32) * 2.0 / values.shape[-1])
    angle = where.astype(jnp.float32)[:, None] * freq[None, :]
    cosine = jnp.cos(angle)[:, None, :]
    sine = jnp.sin(angle)[:, None, :]
    first = values[..., :half]
    second = values[..., half:]
    return jnp.concatenate([first * cosine - second * sine, first * sine + second * cosine], -1)


def per_device(
    x_resid,
    q_new,
    kv_new,
    kv_cache,
    cache_len,
    page_table,
    sinks,
    out_weight,
    norm_gain,
    routes,
    route_wt,
    w_gate,
    w_up,
    w_down,
):
    seq_count = lax.axis_size("seq")
    seq_here = lax.axis_index("seq")
    rows, cols = x_resid.shape
    local_kv = kv_new.shape[1]
    head = kv_new.shape[2] // 2
    local_q = q_new.shape[1] // head
    group = local_q // local_kv
    slots = kv_cache.shape[0]
    page = kv_cache.shape[1]
    requests, max_pages = page_table.shape
    topk = routes.shape[1]
    assert rows == NEW and requests == seq_count and max_pages == seq_count

    length = cache_len[seq_here]
    where = length + jnp.arange(rows, dtype=jnp.int32)
    queries = rotate(q_new.reshape(rows, local_q, head).astype(jnp.float32), where).astype(
        jnp.bfloat16
    )
    fresh_keys = rotate(kv_new[..., :head].astype(jnp.float32), where).astype(jnp.bfloat16)
    fresh_vals = kv_new[..., head:]

    home = page_table // slots
    mine = home == seq_here
    slot_of = jnp.sum(jnp.where(mine, page_table % slots, 0), 1)
    outgoing = kv_cache[slot_of]
    incoming = lax.all_to_all(outgoing, "seq", split_axis=0, concat_axis=0, tiled=True)
    own_home = home[seq_here]
    page_ids = jnp.arange(max_pages, dtype=jnp.int32)
    src_ids = jnp.arange(seq_count, dtype=jnp.int32)
    page_of_src = jnp.sum(
        jnp.where(own_home[None, :] == src_ids[:, None], page_ids[None, :], 0), 1
    )
    spots = page_of_src[:, None] * page + jnp.arange(page, dtype=jnp.int32)[None, :]
    cache_ok = (spots < length).reshape(seq_count * page)
    cache_keys = incoming[..., :head].reshape(seq_count * page, local_kv, head)
    cache_vals = incoming[..., head:].reshape(seq_count * page, local_kv, head)

    q_g = queries.reshape(rows, local_kv, group, head)
    scale = head ** (-0.5)
    s_cache = jnp.einsum(
        "ngqd,kgd->gqnk", q_g, cache_keys, preferred_element_type=jnp.float32
    ) * scale
    s_cache = jnp.where(cache_ok[None, None, None, :], s_cache, neg_big)
    s_new = jnp.einsum(
        "ngqd,kgd->gqnk", q_g, fresh_keys, preferred_element_type=jnp.float32
    ) * scale
    tok = jnp.arange(rows, dtype=jnp.int32)
    causal = tok[None, :] <= tok[:, None]
    s_new = jnp.where(causal[None, None], s_new, neg_big)
    sink = sinks.reshape(local_kv, group)[:, :, None]
    top = jnp.maximum(jnp.maximum(jnp.max(s_cache, -1), jnp.max(s_new, -1)), sink)
    e_cache = jnp.exp(s_cache - top[..., None])
    e_new = jnp.exp(s_new - top[..., None])
    total = jnp.sum(e_cache, -1) + jnp.sum(e_new, -1) + jnp.exp(sink - top)
    summed = jnp.einsum(
        "gqnk,kgd->gqnd", e_cache.astype(jnp.bfloat16), cache_vals,
        preferred_element_type=jnp.float32,
    ) + jnp.einsum(
        "gqnk,kgd->gqnd", e_new.astype(jnp.bfloat16), fresh_vals,
        preferred_element_type=jnp.float32,
    )
    attended = (summed / total[..., None]).astype(jnp.bfloat16)
    attended = attended.transpose(2, 0, 1, 3).reshape(rows, local_q * head)

    partial_value = jnp.dot(attended, out_weight, preferred_element_type=jnp.float32)
    tp_count = D // cols
    blocks = partial_value.astype(jnp.bfloat16).reshape(rows, tp_count, cols).transpose(1, 0, 2)
    blocks = lax.all_to_all(blocks, "tp", split_axis=0, concat_axis=0, tiled=True)
    column_sums = jnp.sum(blocks.astype(jnp.float32), 0)
    resid = (x_resid.astype(jnp.float32) + column_sums).astype(jnp.bfloat16)
    resid_wide = resid.astype(jnp.float32)
    spread = jnp.broadcast_to(resid[None], (tp_count, rows, cols))
    spread = lax.all_to_all(spread, "tp", split_axis=0, concat_axis=0, tiled=True)
    resid_full = spread.transpose(1, 0, 2).reshape(rows, D).astype(jnp.float32)
    squares = jnp.sum(resid_full * resid_full, 1)
    scale_rows = lax.rsqrt(squares / D + norm_eps)
    normed_full = (resid_full * scale_rows[:, None] * norm_gain[None, :]).astype(jnp.bfloat16)

    local_e = w_gate.shape[0]
    experts_all = local_e * seq_count
    cap = 2 * rows * topk // experts_all
    chunks = 2
    part = cap // chunks
    flat_routes = routes.reshape(-1)
    onehot = (flat_routes[:, None] == jnp.arange(experts_all, dtype=jnp.int32)[None, :]).astype(
        jnp.int32
    )
    rank = jnp.sum(onehot * (jnp.cumsum(onehot, 0) - 1), 1)
    slot = (rank // part) * (experts_all * part) + flat_routes * part + rank % part
    source = (
        jnp.full((experts_all * cap,), rows, jnp.int32)
        .at[slot]
        .set(jnp.arange(rows * topk, dtype=jnp.int32) // topk)
    ).reshape(chunks, experts_all * part)
    token_ids = jnp.arange(rows, dtype=jnp.int32)
    w_down_split = w_down.reshape(local_e, w_down.shape[1], tp_count, cols)
    row_major2 = Layout(major_to_minor=(0, 1))
    tp_here = lax.axis_index("tp")
    gain_here = lax.dynamic_slice_in_dim(norm_gain, tp_here * cols, cols)
    normed_own = (resid_wide * scale_rows[:, None] * gain_here[None, :]).astype(jnp.bfloat16)
    w_gate_in = w_gate[0].reshape(tp_count, cols, w_gate.shape[2])
    w_up_in = w_up[0].reshape(tp_count, cols, w_up.shape[2])
    pieces = []
    for c in range(chunks):
        picks = (source[c][:, None] == token_ids[None, :]).astype(jnp.bfloat16)
        if c == 0:
            sent = jnp.dot(picks, normed_full, preferred_element_type=jnp.float32).astype(
                jnp.bfloat16
            )
            sent = with_layout_constraint(sent, row_major2).reshape(seq_count, local_e * part, D)
            arrived = lax.all_to_all(sent, "seq", split_axis=0, concat_axis=0, tiled=True)
            arrived = arrived.reshape(seq_count, local_e, part, D)
            hidden = jnp.einsum(
                "sexd,edf->sexf", arrived, w_gate, preferred_element_type=jnp.float32
            )
            lin = jnp.einsum("sexd,edf->sexf", arrived, w_up, preferred_element_type=jnp.float32)
        else:
            sent = jnp.dot(picks, normed_own, preferred_element_type=jnp.float32).astype(
                jnp.bfloat16
            )
            sent = with_layout_constraint(sent, row_major2).reshape(seq_count, local_e * part, cols)
            arrived = lax.all_to_all(sent, "seq", split_axis=0, concat_axis=0, tiled=True)
            blocks_in = lax.all_gather(
                arrived.reshape(seq_count * local_e * part, cols), "tp", axis=0, tiled=False
            )
            hidden = jnp.einsum(
                "jmk,jkf->mf", blocks_in, w_gate_in, preferred_element_type=jnp.float32
            ).reshape(seq_count, local_e, part, -1)
            lin = jnp.einsum(
                "jmk,jkf->mf", blocks_in, w_up_in, preferred_element_type=jnp.float32
            ).reshape(seq_count, local_e, part, -1)
        act = (hidden * jax.nn.sigmoid(1.702 * hidden) * (lin + 1.0)).astype(jnp.bfloat16)
        down = jnp.einsum(
            "sexf,efjk->jsexk", act, w_down_split, preferred_element_type=jnp.float32
        ).astype(jnp.bfloat16)
        down = with_layout_constraint(down, Layout(major_to_minor=(0, 1, 2, 3, 4)))
        down = down.reshape(tp_count * seq_count * local_e * part, cols)
        expert_out = lax.psum_scatter(down, "tp", scatter_dimension=0, tiled=True)
        back = lax.all_to_all(
            expert_out.reshape(seq_count, local_e * part, cols),
            "seq",
            split_axis=0,
            concat_axis=0,
            tiled=True,
        )
        pieces.append(back)
    returned = jnp.stack(pieces, 0)
    taken = (
        returned.reshape(experts_all * cap, cols)[slot]
        .reshape(rows, topk, cols)
        .astype(jnp.float32)
    )
    mixture = jnp.sum(route_wt[..., None] * taken, 1)
    output = (resid_wide + mixture).astype(jnp.bfloat16)
    return (attended, output)


def solution(mesh):
    in_specs = (
        P("seq", "tp"),
        P("seq", "tp"),
        P("seq", "tp", None),
        P("seq", None, "tp", None),
        P(),
        P(),
        P("tp"),
        P("tp", None),
        P(),
        P("seq", None),
        P("seq", None),
        P("seq", None, "tp"),
        P("seq", None, "tp"),
        P("seq", "tp", None),
    )
    out_specs = (P("seq", "tp"), P("seq", "tp"))
    return jax.shard_map(
        per_device, mesh=mesh, in_specs=in_specs, out_specs=out_specs, check_vma=False
    )
```

```python
import jax
import jax.numpy as jnp
from jax import lax
from jax.experimental.layout import Layout, with_layout_constraint
from jax.sharding import PartitionSpec as P

D = 2880
NEW = 128


rope_base = 150000.0
neg_big = -1e30
norm_eps = 1e-05


def rotate(values, where):
    half = values.shape[-1] // 2
    freq = rope_base ** (-jnp.arange(half, dtype=jnp.float32) * 2.0 / values.shape[-1])
    angle = where.astype(jnp.float32)[:, None] * freq[None, :]
    cosine = jnp.cos(angle)[:, None, :]
    sine = jnp.sin(angle)[:, None, :]
    first = values[..., :half]
    second = values[..., half:]
    return jnp.concatenate([first * cosine - second * sine, first * sine + second * cosine], -1)


def per_device(
    x_resid,
    q_new,
    kv_new,
    kv_cache,
    cache_len,
    page_table,
    sinks,
    out_weight,
    norm_gain,
    routes,
    route_wt,
    w_gate,
    w_up,
    w_down,
):
    seq_count = lax.axis_size("seq")
    seq_here = lax.axis_index("seq")
    rows, cols = x_resid.shape
    local_kv = kv_new.shape[1]
    head = kv_new.shape[2] // 2
    local_q = q_new.shape[1] // head
    group = local_q // local_kv
    slots = kv_cache.shape[0]
    page = kv_cache.shape[1]
    requests, max_pages = page_table.shape
    topk = routes.shape[1]
    assert rows == NEW and requests == seq_count and max_pages == seq_count

    length = cache_len[seq_here]
    where = length + jnp.arange(rows, dtype=jnp.int32)
    queries = rotate(q_new.reshape(rows, local_q, head).astype(jnp.float32), where).astype(
        jnp.bfloat16
    )
    fresh_keys = rotate(kv_new[..., :head].astype(jnp.float32), where).astype(jnp.bfloat16)
    fresh_vals = kv_new[..., head:]

    home = page_table // slots
    mine = home == seq_here
    slot_of = jnp.sum(jnp.where(mine, page_table % slots, 0), 1)
    outgoing = kv_cache[slot_of]
    incoming = lax.all_to_all(outgoing, "seq", split_axis=0, concat_axis=0, tiled=True)
    own_home = home[seq_here]
    page_ids = jnp.arange(max_pages, dtype=jnp.int32)
    src_ids = jnp.arange(seq_count, dtype=jnp.int32)
    page_of_src = jnp.sum(
        jnp.where(own_home[None, :] == src_ids[:, None], page_ids[None, :], 0), 1
    )
    spots = page_of_src[:, None] * page + jnp.arange(page, dtype=jnp.int32)[None, :]
    cache_ok = (spots < length).reshape(seq_count * page)
    cache_keys = incoming[..., :head].reshape(seq_count * page, local_kv, head)
    cache_vals = incoming[..., head:].reshape(seq_count * page, local_kv, head)

    q_g = queries.reshape(rows, local_kv, group, head)
    scale = head ** (-0.5)
    s_cache = jnp.einsum(
        "ngqd,kgd->gqnk", q_g, cache_keys, preferred_element_type=jnp.float32
    ) * scale
    s_cache = jnp.where(cache_ok[None, None, None, :], s_cache, neg_big)
    s_new = jnp.einsum(
        "ngqd,kgd->gqnk", q_g, fresh_keys, preferred_element_type=jnp.float32
    ) * scale
    tok = jnp.arange(rows, dtype=jnp.int32)
    causal = tok[None, :] <= tok[:, None]
    s_new = jnp.where(causal[None, None], s_new, neg_big)
    sink = sinks.reshape(local_kv, group)[:, :, None]
    top = jnp.maximum(jnp.maximum(jnp.max(s_cache, -1), jnp.max(s_new, -1)), sink)
    e_cache = jnp.exp(s_cache - top[..., None])
    e_new = jnp.exp(s_new - top[..., None])
    total = jnp.sum(e_cache, -1) + jnp.sum(e_new, -1) + jnp.exp(sink - top)
    summed = jnp.einsum(
        "gqnk,kgd->gqnd", e_cache.astype(jnp.bfloat16), cache_vals,
        preferred_element_type=jnp.float32,
    ) + jnp.einsum(
        "gqnk,kgd->gqnd", e_new.astype(jnp.bfloat16), fresh_vals,
        preferred_element_type=jnp.float32,
    )
    attended = (summed / total[..., None]).astype(jnp.bfloat16)
    attended = attended.transpose(2, 0, 1, 3).reshape(rows, local_q * head)

    partial_value = jnp.dot(attended, out_weight, preferred_element_type=jnp.float32)
    tp_count = D // cols
    blocks = partial_value.astype(jnp.bfloat16).reshape(rows, tp_count, cols).transpose(1, 0, 2)
    blocks = lax.all_to_all(blocks, "tp", split_axis=0, concat_axis=0, tiled=True)
    column_sums = jnp.sum(blocks.astype(jnp.float32), 0)
    resid = (x_resid.astype(jnp.float32) + column_sums).astype(jnp.bfloat16)
    resid_wide = resid.astype(jnp.float32)
    spread = jnp.broadcast_to(resid[None], (tp_count, rows, cols))
    spread = lax.all_to_all(spread, "tp", split_axis=0, concat_axis=0, tiled=True)
    resid_full = spread.transpose(1, 0, 2).reshape(rows, D).astype(jnp.float32)
    squares = jnp.sum(resid_full * resid_full, 1)
    scale_rows = lax.rsqrt(squares / D + norm_eps)
    normed_full = (resid_full * scale_rows[:, None] * norm_gain[None, :]).astype(jnp.bfloat16)

    local_e = w_gate.shape[0]
    experts_all = local_e * seq_count
    cap = 2 * rows * topk // experts_all
    chunks = 2
    part = cap // chunks
    flat_routes = routes.reshape(-1)
    onehot = (flat_routes[:, None] == jnp.arange(experts_all, dtype=jnp.int32)[None, :]).astype(
        jnp.int32
    )
    rank = jnp.sum(onehot * (jnp.cumsum(onehot, 0) - 1), 1)
    slot = (rank // part) * (experts_all * part) + flat_routes * part + rank % part
    source = (
        jnp.full((experts_all * cap,), rows, jnp.int32)
        .at[slot]
        .set(jnp.arange(rows * topk, dtype=jnp.int32) // topk)
    ).reshape(chunks, experts_all * part)
    token_ids = jnp.arange(rows, dtype=jnp.int32)
    w_down_split = w_down.reshape(local_e, w_down.shape[1], tp_count, cols)
    row_major2 = Layout(major_to_minor=(0, 1))
    tp_here = lax.axis_index("tp")
    gain_here = lax.dynamic_slice_in_dim(norm_gain, tp_here * cols, cols)
    normed_own = (resid_wide * scale_rows[:, None] * gain_here[None, :]).astype(jnp.bfloat16)
    pieces = []
    for c in range(chunks):
        picks = (source[c][:, None] == token_ids[None, :]).astype(jnp.bfloat16)
        if c == 0:
            sent = jnp.dot(picks, normed_full, preferred_element_type=jnp.float32).astype(
                jnp.bfloat16
            )
            sent = with_layout_constraint(sent, row_major2).reshape(seq_count, local_e * part, D)
            arrived = lax.all_to_all(sent, "seq", split_axis=0, concat_axis=0, tiled=True)
            arrived = arrived.reshape(seq_count, local_e, part, D)
            hidden = jnp.einsum(
                "sexd,edf->sexf", arrived, w_gate, preferred_element_type=jnp.float32
            )
            lin = jnp.einsum("sexd,edf->sexf", arrived, w_up, preferred_element_type=jnp.float32)
        else:
            sent = jnp.dot(picks, normed_own, preferred_element_type=jnp.float32).astype(
                jnp.bfloat16
            )
            sent = with_layout_constraint(sent, row_major2).reshape(seq_count, local_e * part, cols)
            arrived = lax.all_to_all(sent, "seq", split_axis=0, concat_axis=0, tiled=True)
            blocks_in = lax.all_gather(
                arrived.reshape(seq_count * local_e * part, cols), "tp", axis=0, tiled=False
            )
            arrived = blocks_in.transpose(1, 0, 2).reshape(seq_count, local_e, part, D)
            hidden = jnp.einsum(
                "sexd,edf->sexf", arrived, w_gate, preferred_element_type=jnp.float32
            )
            lin = jnp.einsum("sexd,edf->sexf", arrived, w_up, preferred_element_type=jnp.float32)
        act = (hidden * jax.nn.sigmoid(1.702 * hidden) * (lin + 1.0)).astype(jnp.bfloat16)
        down = jnp.einsum(
            "sexf,efjk->jsexk", act, w_down_split, preferred_element_type=jnp.float32
        ).astype(jnp.bfloat16)
        down = with_layout_constraint(down, Layout(major_to_minor=(0, 1, 2, 3, 4)))
        down = down.reshape(tp_count * seq_count * local_e * part, cols)
        expert_out = lax.psum_scatter(down, "tp", scatter_dimension=0, tiled=True)
        back = lax.all_to_all(
            expert_out.reshape(seq_count, local_e * part, cols),
            "seq",
            split_axis=0,
            concat_axis=0,
            tiled=True,
        )
        pieces.append(back)
    returned = jnp.stack(pieces, 0)
    taken = (
        returned.reshape(experts_all * cap, cols)[slot]
        .reshape(rows, topk, cols)
        .astype(jnp.float32)
    )
    mixture = jnp.sum(route_wt[..., None] * taken, 1)
    output = (resid_wide + mixture).astype(jnp.bfloat16)
    return (attended, output)


def solution(mesh):
    in_specs = (
        P("seq", "tp"),
        P("seq", "tp"),
        P("seq", "tp", None),
        P("seq", None, "tp", None),
        P(),
        P(),
        P("tp"),
        P("tp", None),
        P(),
        P("seq", None),
        P("seq", None),
        P("seq", None, "tp"),
        P("seq", None, "tp"),
        P("seq", "tp", None),
    )
    out_specs = (P("seq", "tp"), P("seq", "tp"))
    return jax.shard_map(
        per_device, mesh=mesh, in_specs=in_specs, out_specs=out_specs, check_vma=False
    )
```

```python
import jax
import jax.numpy as jnp
from jax import lax
from jax.experimental.layout import Layout, with_layout_constraint
from jax.sharding import PartitionSpec as P

D = 2880
NEW = 128


rope_base = 150000.0
neg_big = -1e30
norm_eps = 1e-05


def rotate(values, where):
    half = values.shape[-1] // 2
    freq = rope_base ** (-jnp.arange(half, dtype=jnp.float32) * 2.0 / values.shape[-1])
    angle = where.astype(jnp.float32)[:, None] * freq[None, :]
    cosine = jnp.cos(angle)[:, None, :]
    sine = jnp.sin(angle)[:, None, :]
    first = values[..., :half]
    second = values[..., half:]
    return jnp.concatenate([first * cosine - second * sine, first * sine + second * cosine], -1)


def per_device(
    x_resid,
    q_new,
    kv_new,
    kv_cache,
    cache_len,
    page_table,
    sinks,
    out_weight,
    norm_gain,
    routes,
    route_wt,
    w_gate,
    w_up,
    w_down,
):
    seq_count = lax.axis_size("seq")
    seq_here = lax.axis_index("seq")
    rows, cols = x_resid.shape
    local_kv = kv_new.shape[1]
    head = kv_new.shape[2] // 2
    local_q = q_new.shape[1] // head
    group = local_q // local_kv
    slots = kv_cache.shape[0]
    page = kv_cache.shape[1]
    requests, max_pages = page_table.shape
    topk = routes.shape[1]
    assert rows == NEW and requests == seq_count and max_pages == seq_count

    length = cache_len[seq_here]
    where = length + jnp.arange(rows, dtype=jnp.int32)
    queries = rotate(q_new.reshape(rows, local_q, head).astype(jnp.float32), where).astype(
        jnp.bfloat16
    )
    fresh_keys = rotate(kv_new[..., :head].astype(jnp.float32), where).astype(jnp.bfloat16)
    fresh_vals = kv_new[..., head:]

    home = page_table // slots
    mine = home == seq_here
    slot_of = jnp.sum(jnp.where(mine, page_table % slots, 0), 1)
    outgoing = kv_cache[slot_of]
    incoming = lax.all_to_all(outgoing, "seq", split_axis=0, concat_axis=0, tiled=True)
    own_home = home[seq_here]
    page_ids = jnp.arange(max_pages, dtype=jnp.int32)
    src_ids = jnp.arange(seq_count, dtype=jnp.int32)
    page_of_src = jnp.sum(
        jnp.where(own_home[None, :] == src_ids[:, None], page_ids[None, :], 0), 1
    )
    spots = page_of_src[:, None] * page + jnp.arange(page, dtype=jnp.int32)[None, :]
    cache_ok = (spots < length).reshape(seq_count * page)
    cache_keys = incoming[..., :head].reshape(seq_count * page, local_kv, head)
    cache_vals = incoming[..., head:].reshape(seq_count * page, local_kv, head)

    q_g = queries.reshape(rows, local_kv, group, head)
    scale = head ** (-0.5)
    s_cache = jnp.einsum(
        "ngqd,kgd->gqnk", q_g, cache_keys, preferred_element_type=jnp.float32
    ) * scale
    s_cache = jnp.where(cache_ok[None, None, None, :], s_cache, neg_big)
    s_new = jnp.einsum(
        "ngqd,kgd->gqnk", q_g, fresh_keys, preferred_element_type=jnp.float32
    ) * scale
    tok = jnp.arange(rows, dtype=jnp.int32)
    causal = tok[None, :] <= tok[:, None]
    s_new = jnp.where(causal[None, None], s_new, neg_big)
    sink = sinks.reshape(local_kv, group)[:, :, None]
    top = jnp.maximum(jnp.maximum(jnp.max(s_cache, -1), jnp.max(s_new, -1)), sink)
    e_cache = jnp.exp(s_cache - top[..., None])
    e_new = jnp.exp(s_new - top[..., None])
    total = jnp.sum(e_cache, -1) + jnp.sum(e_new, -1) + jnp.exp(sink - top)
    summed = jnp.einsum(
        "gqnk,kgd->gqnd", e_cache.astype(jnp.bfloat16), cache_vals,
        preferred_element_type=jnp.float32,
    ) + jnp.einsum(
        "gqnk,kgd->gqnd", e_new.astype(jnp.bfloat16), fresh_vals,
        preferred_element_type=jnp.float32,
    )
    attended = (summed / total[..., None]).astype(jnp.bfloat16)
    attended = attended.transpose(2, 0, 1, 3).reshape(rows, local_q * head)

    partial_value = jnp.dot(attended, out_weight, preferred_element_type=jnp.float32)
    tp_count = D // cols
    blocks = partial_value.astype(jnp.bfloat16).reshape(rows, tp_count, cols).transpose(1, 0, 2)
    blocks = lax.all_to_all(blocks, "tp", split_axis=0, concat_axis=0, tiled=True)
    column_sums = jnp.sum(blocks.astype(jnp.float32), 0)
    resid = (x_resid.astype(jnp.float32) + column_sums).astype(jnp.bfloat16)
    resid_wide = resid.astype(jnp.float32)
    spread = jnp.broadcast_to(resid[None], (tp_count, rows, cols))
    spread = lax.all_to_all(spread, "tp", split_axis=0, concat_axis=0, tiled=True)
    resid_full = spread.transpose(1, 0, 2).reshape(rows, D).astype(jnp.float32)
    squares = jnp.sum(resid_full * resid_full, 1)
    scale_rows = lax.rsqrt(squares / D + norm_eps)
    normed_full = (resid_full * scale_rows[:, None] * norm_gain[None, :]).astype(jnp.bfloat16)

    local_e = w_gate.shape[0]
    experts_all = local_e * seq_count
    cap = 2 * rows * topk // experts_all
    bounds = (0, 20, cap)
    flat_routes = routes.reshape(-1)
    onehot = (flat_routes[:, None] == jnp.arange(experts_all, dtype=jnp.int32)[None, :]).astype(
        jnp.int32
    )
    rank = jnp.sum(onehot * (jnp.cumsum(onehot, 0) - 1), 1)
    slot = jnp.zeros_like(rank)
    for lo, hi in zip(bounds[:-1], bounds[1:]):
        inside = (rank >= lo) & (rank < hi)
        slot = jnp.where(inside, experts_all * lo + flat_routes * (hi - lo) + rank - lo, slot)
    source = (
        jnp.full((experts_all * cap,), rows, jnp.int32)
        .at[slot]
        .set(jnp.arange(rows * topk, dtype=jnp.int32) // topk)
    )
    token_ids = jnp.arange(rows, dtype=jnp.int32)
    w_down_split = w_down.reshape(local_e, w_down.shape[1], tp_count, cols)
    row_major2 = Layout(major_to_minor=(0, 1))
    pieces = []
    for lo, hi in zip(bounds[:-1], bounds[1:]):
        part = hi - lo
        chunk_src = source[experts_all * lo:experts_all * hi]
        picks = (chunk_src[:, None] == token_ids[None, :]).astype(jnp.bfloat16)
        sent = jnp.dot(picks, normed_full, preferred_element_type=jnp.float32).astype(
            jnp.bfloat16
        )
        sent = with_layout_constraint(sent, row_major2).reshape(seq_count, local_e * part, D)
        arrived = lax.all_to_all(sent, "seq", split_axis=0, concat_axis=0, tiled=True)
        arrived = arrived.reshape(seq_count, local_e, part, D)
        hidden = jnp.einsum("sexd,edf->sexf", arrived, w_gate, preferred_element_type=jnp.float32)
        lin = jnp.einsum("sexd,edf->sexf", arrived, w_up, preferred_element_type=jnp.float32)
        act = (hidden * jax.nn.sigmoid(1.702 * hidden) * (lin + 1.0)).astype(jnp.bfloat16)
        down = jnp.einsum(
            "sexf,efjk->jsexk", act, w_down_split, preferred_element_type=jnp.float32
        ).astype(jnp.bfloat16)
        down = with_layout_constraint(down, Layout(major_to_minor=(0, 1, 2, 3, 4)))
        down = down.reshape(tp_count * seq_count * local_e * part, cols)
        expert_out = lax.psum_scatter(down, "tp", scatter_dimension=0, tiled=True)
        back = lax.all_to_all(
            expert_out.reshape(seq_count, local_e * part, cols),
            "seq",
            split_axis=0,
            concat_axis=0,
            tiled=True,
        )
        pieces.append(back)
    returned = jnp.concatenate([p.reshape(-1, cols) for p in pieces], 0)
    taken = returned[slot].reshape(rows, topk, cols).astype(jnp.float32)
    mixture = jnp.sum(route_wt[..., None] * taken, 1)
    output = (resid_wide + mixture).astype(jnp.bfloat16)
    return (attended, output)


def solution(mesh):
    in_specs = (
        P("seq", "tp"),
        P("seq", "tp"),
        P("seq", "tp", None),
        P("seq", None, "tp", None),
        P(),
        P(),
        P("tp"),
        P("tp", None),
        P(),
        P("seq", None),
        P("seq", None),
        P("seq", None, "tp"),
        P("seq", None, "tp"),
        P("seq", "tp", None),
    )
    out_specs = (P("seq", "tp"), P("seq", "tp"))
    return jax.shard_map(
        per_device, mesh=mesh, in_specs=in_specs, out_specs=out_specs, check_vma=False
    )
```
